128 devices in a mesh: rep: 8 (over z_hi, x), shard: 16 (over y, z_lo, core).
Axes of the slice: x: 4, y: 4, z: 4 (z_hi: 2, z_lo: 2; z = z_hi * 2 + z_lo), core: 2. Of those that a mesh axis runs over, the one named last changes fastest.
Arguments:
- inner_wqkv: float32 [8, 2048, 4096], P('rep', 'shard'), may hold values from -8.5 to 8.5
- inner_w1: float32 [8, 2048, 6144], P('rep', 'shard'), may hold values from -8.5 to 8.5
- inner_w3: float32 [8, 2048, 6144], P('rep', 'shard'), may hold values from -8.5 to 8.5
- inner_wo: float32 [8, 2048, 2048], P('rep', 'shard'), may hold values from -8.5 to 8.5
- inner_w2: float32 [8, 6144, 2048], P('rep', 'shard'), may hold values from -8.5 to 8.5
- outer_wqkv: float32 [2048, 4096], P('shard', 'rep'), may hold values from -8 to 8
- outer_w1: float32 [2048, 6144], P('shard', 'rep'), may hold values from -8 to 8
- outer_w3: float32 [2048, 6144], P('shard', 'rep'), may hold values from -8 to 8
- outer_wo: float32 [2048, 2048], P('shard', 'rep'), may hold values from -8 to 8
- outer_w2: float32 [6144, 2048], P('shard', 'rep'), may hold values from -8 to 8
- moment_wqkv: float32 [2048, 4096], P('shard', 'rep'), may hold values from -0.4 to 0.4
- moment_w1: float32 [2048, 6144], P('shard', 'rep'), may hold values from -0.4 to 0.4
- moment_w3: float32 [2048, 6144], P('shard', 'rep'), may hold values from -0.4 to 0.4
- moment_wo: float32 [2048, 2048], P('shard', 'rep'), may hold values from -0.4 to 0.4
- moment_w2: float32 [6144, 2048], P('shard', 'rep'), may hold values from -0.4 to 0.4
- basis_wo: float32 [2048, 64], P('shard'), may hold values from -0.5 to 0.5
- basis_w2: float32 [6144, 64], P('shard'), may hold values from -0.3125 to 0.3125
Outputs:
- weights_wqkv: bfloat16 [2048, 4096], P('shard')
- weights_w1: bfloat16 [2048, 6144], P('shard')
- weights_w3: bfloat16 [2048, 6144], P('shard')
- weights_wo: bfloat16 [2048, 2048], P('shard')
- weights_w2: bfloat16 [6144, 2048], P('shard')
- master_wqkv: float32 [2048, 4096], P('shard', 'rep')
- master_w1: float32 [2048, 6144], P('shard', 'rep')
- master_w3: float32 [2048, 6144], P('shard', 'rep')
- master_wo: float32 [2048, 2048], P('shard', 'rep')
- master_w2: float32 [6144, 2048], P('shard', 'rep')
- momentum_wqkv: float32 [2048, 4096], P('shard', 'rep')
- momentum_w1: float32 [2048, 6144], P('shard', 'rep')
- momentum_w3: float32 [2048, 6144], P('shard', 'rep')
- momentum_wo: float32 [2048, 2048], P('shard', 'rep')
- momentum_w2: float32 [6144, 2048], P('shard', 'rep')
The draws below stay inside these ranges and needn't reach their ends.
All inputs are finite; a program needn't handle non-finite values.
Results may differ from the reference program's by a relative error of at most 0.007.
Values may be sent and summed in bfloat16 or wider, within the bound.
No kernel may reach another device: no remote copies, remote signals or barrier semaphores. Data moves between devices by JAX's collectives and lax.ppermute only.
A program may use at most 128 MiB of HBM per device.

```python
import jax
import jax.numpy as jnp
from jax import lax

D = 2048
FF = 6144
RANK = 64
QKV = 4096
GROUPS = 8
N_REP = 8


def outer_field(key, salt, row_count, col_count):
    sub = jax.random.fold_in(key, salt)
    values = jnp.clip(3.0 * jax.random.normal(sub, (row_count, col_count), jnp.float32), -8.0, 8.0)
    return values


def inner_field(key, salt, row_count, col_count):
    base = outer_field(key, salt, row_count, col_count)
    sub = jax.random.fold_in(key, salt + 100)
    noise = jnp.clip(0.1 * jax.random.normal(sub, (GROUPS, row_count, col_count), jnp.float32), -0.5, 0.5)
    return base[None, :, :] + noise


def draw_outer_wqkv(key, part):
    return outer_field(key, 1, D, QKV)


def draw_outer_w1(key, part):
    return outer_field(key, 2, D, FF)


def draw_outer_w3(key, part):
    return outer_field(key, 3, D, FF)


def draw_outer_wo(key, part):
    return outer_field(key, 4, D, D)


def draw_outer_w2(key, part):
    return outer_field(key, 5, FF, D)


def draw_inner_wqkv(key, part):
    return inner_field(key, 1, D, QKV)


def draw_inner_w1(key, part):
    return inner_field(key, 2, D, FF)


def draw_inner_w3(key, part):
    return inner_field(key, 3, D, FF)


def draw_inner_wo(key, part):
    return inner_field(key, 4, D, D)


def draw_inner_w2(key, part):
    return inner_field(key, 5, FF, D)


def levels(rng, shape, split, low, high):
    loudness = 1.0
    for axis_at, blocks in split:
        draws = jax.random.uniform(jax.random.fold_in(jax.random.fold_in(rng, 6), axis_at), (blocks,), jnp.float32, low / len(split), high / len(split))
        loudness = loudness * jnp.repeat(jnp.exp(draws), shape[axis_at] // blocks).reshape((-1,) + (1,) * (len(shape) - 1 - axis_at))
    return loudness


def centred(key, shape, scale, limit, shards=(), dtype=jnp.bfloat16):
    result = scale * jax.random.normal(key, shape, jnp.float32)
    if shards:
        result = result * levels(key, shape, shards, -0.22, 0.18)
    return jnp.clip(result, -limit, limit).astype(dtype)


def setup_inputs(seed: int = 0) -> dict:
    splits = jax.random.split(jax.random.key(seed), 18)
    return {
        "inner_wqkv": draw_inner_wqkv(jax.random.fold_in(splits[17], 71), 0),
        "inner_w1": draw_inner_w1(jax.random.fold_in(splits[17], 71), 0),
        "inner_w3": draw_inner_w3(jax.random.fold_in(splits[17], 71), 0),
        "inner_wo": draw_inner_wo(jax.random.fold_in(splits[17], 71), 0),
        "inner_w2": draw_inner_w2(jax.random.fold_in(splits[17], 71), 0),
        "outer_wqkv": draw_outer_wqkv(jax.random.fold_in(splits[17], 71), 0),
        "outer_w1": draw_outer_w1(jax.random.fold_in(splits[17], 71), 0),
        "outer_w3": draw_outer_w3(jax.random.fold_in(splits[17], 71), 0),
        "outer_wo": draw_outer_wo(jax.random.fold_in(splits[17], 71), 0),
        "outer_w2": draw_outer_w2(jax.random.fold_in(splits[17], 71), 0),
        "moment_wqkv": centred(splits[10], (D, QKV), 0.1, 0.4, ((0, 16), (1, 8)), jnp.float32),
        "moment_w1": centred(splits[11], (D, FF), 0.1, 0.4, ((0, 16), (1, 8)), jnp.float32),
        "moment_w3": centred(splits[12], (D, FF), 0.1, 0.4, ((0, 16), (1, 8)), jnp.float32),
        "moment_wo": centred(splits[13], (D, D), 0.1, 0.4, ((0, 16), (1, 8)), jnp.float32),
        "moment_w2": centred(splits[14], (FF, D), 0.1, 0.4, ((0, 16), (1, 8)), jnp.float32),
        "basis_wo": centred(splits[15], (D, RANK), (D // 16) ** -0.5, 0.5, ((0, 16),), jnp.float32),
        "basis_w2": centred(splits[16], (FF, RANK), (FF // 16) ** -0.5, 0.3125, ((0, 16),), jnp.float32),
    }


rate_outer = 0.7
decay_moment = 0.9


def nesterov(outer, moment, delta):
    moment_new = decay_moment * moment + delta
    master = outer - rate_outer * (delta + decay_moment * moment_new)
    return master.astype(jnp.bfloat16), master, moment_new


def lowrank(inner, outer, basis):
    highest = lax.Precision.HIGHEST
    diff = outer - jnp.sum(inner, axis=0) / N_REP
    coeff = jnp.dot(basis.T, diff, precision=highest, preferred_element_type=jnp.float32)
    return jnp.dot(basis, coeff, precision=highest, preferred_element_type=jnp.float32)


def reference(inner_wqkv, inner_w1, inner_w3, inner_wo, inner_w2, outer_wqkv, outer_w1, outer_w3, outer_wo, outer_w2, moment_wqkv, moment_w1, moment_w3, moment_wo, moment_w2, basis_wo, basis_w2):
    d_qkv = outer_wqkv - jnp.sum(inner_wqkv, axis=0) / N_REP
    d_one = outer_w1 - jnp.sum(inner_w1, axis=0) / N_REP
    d_three = outer_w3 - jnp.sum(inner_w3, axis=0) / N_REP
    d_out = lowrank(inner_wo, outer_wo, basis_wo)
    d_down = lowrank(inner_w2, outer_w2, basis_w2)
    a0, b0, c0 = nesterov(outer_wqkv, moment_wqkv, d_qkv)
    a1, b1, c1 = nesterov(outer_w1, moment_w1, d_one)
    a3, b3, c3 = nesterov(outer_w3, moment_w3, d_three)
    ao, bo, co = nesterov(outer_wo, moment_wo, d_out)
    a2, b2, c2 = nesterov(outer_w2, moment_w2, d_down)
    return (a0, a1, a3, ao, a2, b0, b1, b3, bo, b2, c0, c1, c3, co, c2)
```

```python
import jax
import jax.numpy as jnp
from jax import lax
from jax.sharding import PartitionSpec as P

rate_outer = 0.7
decay_moment = 0.9


def project(basis, matrix):
    return lax.dot_general(
        basis,
        matrix,
        (((0,), (0,)), ((), ())),
        precision=lax.Precision.HIGHEST,
        preferred_element_type=jnp.float32,
    )


def rebuild(basis, coeff):
    return jnp.dot(
        basis, coeff, precision=lax.Precision.HIGHEST, preferred_element_type=jnp.float32
    )


def nesterov(outer, moment, delta):
    moment_new = decay_moment * moment + delta
    master = outer - rate_outer * (delta + decay_moment * moment_new)
    return (master.astype(jnp.bfloat16), master, moment_new)


def by_owner(a, n):
    r, c = a.shape
    return a.reshape(r, n, c // n).transpose(1, 0, 2)


def from_owners(g):
    n, r, w = g.shape
    return g.transpose(1, 0, 2).reshape(r, n * w)


def gather_rep(y, n):
    return lax.all_to_all(jnp.broadcast_to(y[None], (n,) + y.shape), "rep", 0, 0, tiled=True)


def on_device(
    inner_wqkv,
    inner_w1,
    inner_w3,
    inner_wo,
    inner_w2,
    outer_wqkv,
    outer_w1,
    outer_w3,
    outer_wo,
    outer_w2,
    moment_wqkv,
    moment_w1,
    moment_w3,
    moment_wo,
    moment_w2,
    basis_wo,
    basis_w2,
):
    n = lax.axis_size("rep")
    w_qkv = outer_wqkv.shape[1]
    w_ff = outer_w1.shape[1]
    w_o = outer_wo.shape[1]
    w_2 = outer_w2.shape[1]
    rows = inner_wqkv.shape[1]
    rank = basis_wo.shape[1]
    width = w_qkv + 2 * w_ff

    coef_part = jnp.concatenate(
        [by_owner(project(basis_wo, inner_wo[0]), n), by_owner(project(basis_w2, inner_w2[0]), n)],
        axis=2,
    )
    dense = jnp.concatenate(
        [by_owner(inner_wqkv[0], n), by_owner(inner_w1[0], n), by_owner(inner_w3[0], n)], axis=2
    )
    send = jnp.concatenate([dense, coef_part.reshape(n, -1, width)], axis=1)
    total = jnp.sum(lax.all_to_all(send, "rep", 0, 0, tiled=True), axis=0)

    summed = total[:rows]
    own = jnp.concatenate([project(basis_wo, outer_wo), project(basis_w2, outer_w2)], axis=1)
    coeff = lax.psum(own - total[rows:].reshape(rank, w_o + w_2) / n, "shard")

    d_qkv = outer_wqkv - summed[:, :w_qkv] / n
    d_one = outer_w1 - summed[:, w_qkv : w_qkv + w_ff] / n
    d_three = outer_w3 - summed[:, w_qkv + w_ff :] / n
    a0, b0, c0 = nesterov(outer_wqkv, moment_wqkv, d_qkv)
    a1, b1, c1 = nesterov(outer_w1, moment_w1, d_one)
    a3, b3, c3 = nesterov(outer_w3, moment_w3, d_three)
    dense_w = gather_rep(jnp.concatenate([a0, a1, a3], axis=1), n)

    d_out = rebuild(basis_wo, coeff[:, :w_o])
    d_down = rebuild(basis_w2, coeff[:, w_o:])
    ao, bo, co = nesterov(outer_wo, moment_wo, d_out)
    a2, b2, c2 = nesterov(outer_w2, moment_w2, d_down)
    low_w = gather_rep(jnp.concatenate([ao, a2.reshape(rows, -1)], axis=1), n)

    weights_wqkv = from_owners(dense_w[:, :, :w_qkv])
    weights_w1 = from_owners(dense_w[:, :, w_qkv : w_qkv + w_ff])
    weights_w3 = from_owners(dense_w[:, :, w_qkv + w_ff :])
    weights_wo = from_owners(low_w[:, :, :w_o])
    weights_w2 = from_owners(low_w[:, :, w_o:].reshape(n, -1, w_2))
    return (
        weights_wqkv,
        weights_w1,
        weights_w3,
        weights_wo,
        weights_w2,
        b0,
        b1,
        b3,
        bo,
        b2,
        c0,
        c1,
        c3,
        co,
        c2,
    )


def solution(mesh):
    return jax.shard_map(
        on_device,
        mesh=mesh,
        in_specs=(
            P("rep", "shard", None),
            P("rep", "shard", None),
            P("rep", "shard", None),
            P("rep", "shard", None),
            P("rep", "shard", None),
            P("shard", "rep"),
            P("shard", "rep"),
            P("shard", "rep"),
            P("shard", "rep"),
            P("shard", "rep"),
            P("shard", "rep"),
            P("shard", "rep"),
            P("shard", "rep"),
            P("shard", "rep"),
            P("shard", "rep"),
            P("shard", None),
            P("shard", None),
        ),
        out_specs=(
            P("shard", None),
            P("shard", None),
            P("shard", None),
            P("shard", None),
            P("shard", None),
            P("shard", "rep"),
            P("shard", "rep"),
            P("shard", "rep"),
            P("shard", "rep"),
            P("shard", "rep"),
            P("shard", "rep"),
            P("shard", "rep"),
            P("shard", "rep"),
            P("shard", "rep"),
            P("shard", "rep"),
        ),
        check_vma=False,
    )
```

```python
import jax
import jax.numpy as jnp
from jax import lax
from jax.sharding import PartitionSpec as P

rate_outer = 0.7
decay_moment = 0.9


def project(basis, matrix):
    return lax.dot_general(
        basis,
        matrix,
        (((0,), (0,)), ((), ())),
        precision=lax.Precision.HIGHEST,
        preferred_element_type=jnp.float32,
    )


def rebuild(basis, coeff):
    return jnp.dot(
        basis, coeff, precision=lax.Precision.HIGHEST, preferred_element_type=jnp.float32
    )


def nesterov(outer, moment, delta):
    moment_new = decay_moment * moment + delta
    master = outer - rate_outer * (delta + decay_moment * moment_new)
    return (master.astype(jnp.bfloat16), master, moment_new)


def owner_blocks(a, n):
    w = a.shape[1] // n
    return [a[:, j * w : (j + 1) * w] for j in range(n)]


def gather_all(y, axis_name, n):
    return lax.all_to_all(jnp.broadcast_to(y[None], (n,) + y.shape), axis_name, 0, 0, tiled=True)


def on_device(
    inner_wqkv,
    inner_w1,
    inner_w3,
    inner_wo,
    inner_w2,
    outer_wqkv,
    outer_w1,
    outer_w3,
    outer_wo,
    outer_w2,
    moment_wqkv,
    moment_w1,
    moment_w3,
    moment_wo,
    moment_w2,
    basis_wo,
    basis_w2,
):
    n = lax.axis_size("rep")
    n_shard = lax.axis_size("shard")
    w_qkv = outer_wqkv.shape[1]
    w_ff = outer_w1.shape[1]
    w_o = outer_wo.shape[1]
    w_2 = outer_w2.shape[1]
    rows = inner_wqkv.shape[1]
    rows_2 = outer_w2.shape[0]
    rank = basis_wo.shape[1]
    width = w_qkv + 2 * w_ff
    w_c = w_o + w_2
    k_c = width // w_c
    r_c = rank // k_c

    qkv_b = owner_blocks(inner_wqkv[0], n)
    one_b = owner_blocks(inner_w1[0], n)
    three_b = owner_blocks(inner_w3[0], n)
    po_b = owner_blocks(project(basis_wo, inner_wo[0]), n)
    p2_b = owner_blocks(project(basis_w2, inner_w2[0]), n)
    send = []
    for j in range(n):
        part = jnp.concatenate([po_b[j], p2_b[j]], axis=1)
        folded = jnp.concatenate([part[k * r_c : (k + 1) * r_c] for k in range(k_c)], axis=1)
        dense = jnp.concatenate([qkv_b[j], one_b[j], three_b[j]], axis=1)
        send.append(jnp.concatenate([dense, folded], axis=0))
    total = jnp.sum(lax.all_to_all(jnp.stack(send), "rep", 0, 0, tiled=True), axis=0)

    summed = total[:rows]
    folded = total[rows:]
    part = jnp.concatenate([folded[:, k * w_c : (k + 1) * w_c] for k in range(k_c)], axis=0)
    own = jnp.concatenate([project(basis_wo, outer_wo), project(basis_w2, outer_w2)], axis=1)
    coeff = jnp.sum(gather_all(own - part / n, "shard", n_shard), axis=0)

    d_qkv = outer_wqkv - summed[:, :w_qkv] / n
    d_one = outer_w1 - summed[:, w_qkv : w_qkv + w_ff] / n
    d_three = outer_w3 - summed[:, w_qkv + w_ff :] / n
    a0, b0, c0 = nesterov(outer_wqkv, moment_wqkv, d_qkv)
    a1, b1, c1 = nesterov(outer_w1, moment_w1, d_one)
    a3, b3, c3 = nesterov(outer_w3, moment_w3, d_three)
    d_out = rebuild(basis_wo, coeff[:, :w_o])
    d_down = rebuild(basis_w2, coeff[:, w_o:])
    ao, bo, co = nesterov(outer_wo, moment_wo, d_out)
    a2, b2, c2 = nesterov(outer_w2, moment_w2, d_down)

    q = rows_2 // rows
    mine = jnp.concatenate(
        [a0, a1, a3, ao] + [a2[k * rows : (k + 1) * rows] for k in range(q)], axis=1
    )
    got = gather_all(mine, "rep", n)
    o1 = w_qkv
    o3 = o1 + w_ff
    oo = o3 + w_ff
    o2 = oo + w_o
    weights_wqkv = jnp.concatenate([got[j, :, :o1] for j in range(n)], axis=1)
    weights_w1 = jnp.concatenate([got[j, :, o1:o3] for j in range(n)], axis=1)
    weights_w3 = jnp.concatenate([got[j, :, o3:oo] for j in range(n)], axis=1)
    weights_wo = jnp.concatenate([got[j, :, oo:o2] for j in range(n)], axis=1)
    weights_w2 = jnp.concatenate(
        [
            jnp.concatenate(
                [got[j, :, o2 + k * w_2 : o2 + (k + 1) * w_2] for k in range(q)], axis=0
            )
            for j in range(n)
        ],
        axis=1,
    )
    return (
        weights_wqkv,
        weights_w1,
        weights_w3,
        weights_wo,
        weights_w2,
        b0,
        b1,
        b3,
        bo,
        b2,
        c0,
        c1,
        c3,
        co,
        c2,
    )


def solution(mesh):
    return jax.shard_map(
        on_device,
        mesh=mesh,
        in_specs=(
            P("rep", "shard", None),
            P("rep", "shard", None),
            P("rep", "shard", None),
            P("rep", "shard", None),
            P("rep", "shard", None),
            P("shard", "rep"),
            P("shard", "rep"),
            P("shard", "rep"),
            P("shard", "rep"),
            P("shard", "rep"),
            P("shard", "rep"),
            P("shard", "rep"),
            P("shard", "rep"),
            P("shard", "rep"),
            P("shard", "rep"),
            P("shard", None),
            P("shard", None),
        ),
        out_specs=(
            P("shard", None),
            P("shard", None),
            P("shard", None),
            P("shard", None),
            P("shard", None),
            P("shard", "rep"),
            P("shard", "rep"),
            P("shard", "rep"),
            P("shard", "rep"),
            P("shard", "rep"),
            P("shard", "rep"),
            P("shard", "rep"),
            P("shard", "rep"),
            P("shard", "rep"),
            P("shard", "rep"),
        ),
        check_vma=False,
    )
```

```python
import jax
import jax.numpy as jnp
from jax import lax
from jax.sharding import PartitionSpec as P

rate_outer = 0.7
decay_moment = 0.9


def project(basis, matrix):
    return lax.dot_general(
        basis,
        matrix,
        (((0,), (0,)), ((), ())),
        precision=lax.Precision.HIGHEST,
        preferred_element_type=jnp.float32,
    )


def rebuild(basis, coeff):
    return jnp.dot(
        basis, coeff, precision=lax.Precision.HIGHEST, preferred_element_type=jnp.float32
    )


def nesterov(outer, moment, delta):
    moment_new = decay_moment * moment + delta
    master = outer - rate_outer * (delta + decay_moment * moment_new)
    return (master.astype(jnp.bfloat16), master, moment_new)


def owner_blocks(a, n):
    w = a.shape[1] // n
    return [a[:, j * w : (j + 1) * w] for j in range(n)]


def gather_all(y, axis_name, n):
    return lax.all_to_all(jnp.broadcast_to(y[None], (n,) + y.shape), axis_name, 0, 0, tiled=True)


def on_device(
    inner_wqkv,
    inner_w1,
    inner_w3,
    inner_wo,
    inner_w2,
    outer_wqkv,
    outer_w1,
    outer_w3,
    outer_wo,
    outer_w2,
    moment_wqkv,
    moment_w1,
    moment_w3,
    moment_wo,
    moment_w2,
    basis_wo,
    basis_w2,
):
    n = lax.axis_size("rep")
    w_qkv = outer_wqkv.shape[1]
    w_ff = outer_w1.shape[1]
    w_o = outer_wo.shape[1]
    w_2 = outer_w2.shape[1]
    rows = inner_wqkv.shape[1]
    rows_2 = outer_w2.shape[0]
    rank = basis_wo.shape[1]
    width = w_qkv + 2 * w_ff
    w_c = w_o + w_2
    k_c = width // w_c
    r_c = rank // k_c

    qkv_b = owner_blocks(inner_wqkv[0], n)
    one_b = owner_blocks(inner_w1[0], n)
    three_b = owner_blocks(inner_w3[0], n)
    po_b = owner_blocks(project(basis_wo, inner_wo[0]), n)
    p2_b = owner_blocks(project(basis_w2, inner_w2[0]), n)
    send = []
    for j in range(n):
        part = jnp.concatenate([po_b[j], p2_b[j]], axis=1)
        folded = jnp.concatenate([part[k * r_c : (k + 1) * r_c] for k in range(k_c)], axis=1)
        dense = jnp.concatenate([qkv_b[j], one_b[j], three_b[j]], axis=1)
        send.append(jnp.concatenate([dense, folded], axis=0))
    total = jnp.sum(lax.all_to_all(jnp.stack(send), "rep", 0, 0, tiled=True), axis=0)

    summed = total[:rows]
    folded = total[rows:]
    part = jnp.concatenate([folded[:, k * w_c : (k + 1) * w_c] for k in range(k_c)], axis=0)
    own = jnp.concatenate([project(basis_wo, outer_wo), project(basis_w2, outer_w2)], axis=1)
    coeff = jnp.sum(lax.all_gather(own - part / n, "shard", axis=0, tiled=False), axis=0)

    d_qkv = outer_wqkv - summed[:, :w_qkv] / n
    d_one = outer_w1 - summed[:, w_qkv : w_qkv + w_ff] / n
    d_three = outer_w3 - summed[:, w_qkv + w_ff :] / n
    a0, b0, c0 = nesterov(outer_wqkv, moment_wqkv, d_qkv)
    a1, b1, c1 = nesterov(outer_w1, moment_w1, d_one)
    a3, b3, c3 = nesterov(outer_w3, moment_w3, d_three)
    d_out = rebuild(basis_wo, coeff[:, :w_o])
    d_down = rebuild(basis_w2, coeff[:, w_o:])
    ao, bo, co = nesterov(outer_wo, moment_wo, d_out)
    a2, b2, c2 = nesterov(outer_w2, moment_w2, d_down)

    dense_w = gather_all(jnp.concatenate([a0, a1, a3], axis=1), "rep", n)
    q = rows_2 // rows
    low_w = gather_all(
        jnp.concatenate([ao] + [a2[k * rows : (k + 1) * rows] for k in range(q)], axis=1), "rep", n
    )
    o1 = w_qkv
    o3 = o1 + w_ff
    weights_wqkv = jnp.concatenate([dense_w[j, :, :o1] for j in range(n)], axis=1)
    weights_w1 = jnp.concatenate([dense_w[j, :, o1:o3] for j in range(n)], axis=1)
    weights_w3 = jnp.concatenate([dense_w[j, :, o3:] for j in range(n)], axis=1)
    weights_wo = jnp.concatenate([low_w[j, :, :w_o] for j in range(n)], axis=1)
    weights_w2 = jnp.concatenate(
        [
            jnp.concatenate(
                [low_w[j, :, w_o + k * w_2 : w_o + (k + 1) * w_2] for k in range(q)], axis=0
            )
            for j in range(n)
        ],
        axis=1,
    )
    return (
        weights_wqkv,
        weights_w1,
        weights_w3,
        weights_wo,
        weights_w2,
        b0,
        b1,
        b3,
        bo,
        b2,
        c0,
        c1,
        c3,
        co,
        c2,
    )


def solution(mesh):
    return jax.shard_map(
        on_device,
        mesh=mesh,
        in_specs=(
            P("rep", "shard", None),
            P("rep", "shard", None),
            P("rep", "shard", None),
            P("rep", "shard", None),
            P("rep", "shard", None),
            P("shard", "rep"),
            P("shard", "rep"),
            P("shard", "rep"),
            P("shard", "rep"),
            P("shard", "rep"),
            P("shard", "rep"),
            P("shard", "rep"),
            P("shard", "rep"),
            P("shard", "rep"),
            P("shard", "rep"),
            P("shard", None),
            P("shard", None),
        ),
        out_specs=(
            P("shard", None),
            P("shard", None),
            P("shard", None),
            P("shard", None),
            P("shard", None),
            P("shard", "rep"),
            P("shard", "rep"),
            P("shard", "rep"),
            P("shard", "rep"),
            P("shard", "rep"),
            P("shard", "rep"),
            P("shard", "rep"),
            P("shard", "rep"),
            P("shard", "rep"),
            P("shard", "rep"),
        ),
        check_vma=False,
    )
```

```python
import jax
import jax.numpy as jnp
from jax import lax
from jax.sharding import PartitionSpec as P

rate_outer = 0.7
decay_moment = 0.9


def project(basis, matrix):
    return lax.dot_general(
        basis,
        matrix,
        (((0,), (0,)), ((), ())),
        precision=lax.Precision.HIGHEST,
        preferred_element_type=jnp.float32,
    )


def rebuild(basis, coeff):
    return jnp.dot(
        basis, coeff, precision=lax.Precision.HIGHEST, preferred_element_type=jnp.float32
    )


def nesterov(outer, moment, delta):
    moment_new = decay_moment * moment + delta
    master = outer - rate_outer * (delta + decay_moment * moment_new)
    return (master.astype(jnp.bfloat16), master, moment_new)


def owner_blocks(a, n):
    w = a.shape[1] // n
    return [a[:, j * w : (j + 1) * w] for j in range(n)]


def gather_all(y, axis_name, n):
    return lax.all_to_all(jnp.broadcast_to(y[None], (n,) + y.shape), axis_name, 0, 0, tiled=True)


def on_device(
    inner_wqkv,
    inner_w1,
    inner_w3,
    inner_wo,
    inner_w2,
    outer_wqkv,
    outer_w1,
    outer_w3,
    outer_wo,
    outer_w2,
    moment_wqkv,
    moment_w1,
    moment_w3,
    moment_wo,
    moment_w2,
    basis_wo,
    basis_w2,
):
    n = lax.axis_size("rep")
    w_qkv = outer_wqkv.shape[1]
    w_ff = outer_w1.shape[1]
    w_o = outer_wo.shape[1]
    w_2 = outer_w2.shape[1]
    rows = inner_wqkv.shape[1]
    rows_2 = outer_w2.shape[0]

    s_qkv = lax.psum_scatter(
        jnp.stack(owner_blocks(inner_wqkv[0], n)), "rep", scatter_dimension=0, tiled=True
    )[0]
    width = 2 * w_ff
    w_c = w_o + w_2
    k_c = width // w_c
    rank = basis_wo.shape[1]
    r_c = -(-rank // (8 * k_c)) * 8
    one_b = owner_blocks(inner_w1[0], n)
    three_b = owner_blocks(inner_w3[0], n)
    po_b = owner_blocks(project(basis_wo, inner_wo[0]), n)
    p2_b = owner_blocks(project(basis_w2, inner_w2[0]), n)
    send = []
    for j in range(n):
        part = jnp.concatenate([po_b[j], p2_b[j]], axis=1)
        part = jnp.pad(part, ((0, k_c * r_c - rank), (0, 0)))
        folded = jnp.concatenate([part[k * r_c : (k + 1) * r_c] for k in range(k_c)], axis=1)
        dense = jnp.concatenate([one_b[j], three_b[j]], axis=1)
        send.append(jnp.concatenate([dense, folded], axis=0))
    total = jnp.sum(lax.all_to_all(jnp.stack(send), "rep", 0, 0, tiled=True), axis=0)

    summed = total[:rows]
    folded = total[rows:]
    part = jnp.concatenate([folded[:, k * w_c : (k + 1) * w_c] for k in range(k_c)], axis=0)[:rank]
    own = jnp.concatenate([project(basis_wo, outer_wo), project(basis_w2, outer_w2)], axis=1)
    coeff = jnp.sum(lax.all_gather(own - part / n, "shard", axis=0, tiled=False), axis=0)

    d_qkv = outer_wqkv - s_qkv / n
    d_one = outer_w1 - summed[:, :w_ff] / n
    d_three = outer_w3 - summed[:, w_ff:] / n
    a0, b0, c0 = nesterov(outer_wqkv, moment_wqkv, d_qkv)
    a1, b1, c1 = nesterov(outer_w1, moment_w1, d_one)
    a3, b3, c3 = nesterov(outer_w3, moment_w3, d_three)
    d_out = rebuild(basis_wo, coeff[:, :w_o])
    d_down = rebuild(basis_w2, coeff[:, w_o:])
    ao, bo, co = nesterov(outer_wo, moment_wo, d_out)
    a2, b2, c2 = nesterov(outer_w2, moment_w2, d_down)

    dense_w = gather_all(jnp.concatenate([a0, a1, a3], axis=1), "rep", n)
    q = rows_2 // rows
    low_w = gather_all(
        jnp.concatenate([ao] + [a2[k * rows : (k + 1) * rows] for k in range(q)], axis=1), "rep", n
    )
    o1 = w_qkv
    o3 = o1 + w_ff
    weights_wqkv = jnp.concatenate([dense_w[j, :, :o1] for j in range(n)], axis=1)
    weights_w1 = jnp.concatenate([dense_w[j, :, o1:o3] for j in range(n)], axis=1)
    weights_w3 = jnp.concatenate([dense_w[j, :, o3:] for j in range(n)], axis=1)
    weights_wo = jnp.concatenate([low_w[j, :, :w_o] for j in range(n)], axis=1)
    weights_w2 = jnp.concatenate(
        [
            jnp.concatenate(
                [low_w[j, :, w_o + k * w_2 : w_o + (k + 1) * w_2] for k in range(q)], axis=0
            )
            for j in range(n)
        ],
        axis=1,
    )
    return (
        weights_wqkv,
        weights_w1,
        weights_w3,
        weights_wo,
        weights_w2,
        b0,
        b1,
        b3,
        bo,
        b2,
        c0,
        c1,
        c3,
        co,
        c2,
    )


def solution(mesh):
    return jax.shard_map(
        on_device,
        mesh=mesh,
        in_specs=(
            P("rep", "shard", None),
            P("rep", "shard", None),
            P("rep", "shard", None),
            P("rep", "shard", None),
            P("rep", "shard", None),
            P("shard", "rep"),
            P("shard", "rep"),
            P("shard", "rep"),
            P("shard", "rep"),
            P("shard", "rep"),
            P("shard", "rep"),
            P("shard", "rep"),
            P("shard", "rep"),
            P("shard", "rep"),
            P("shard", "rep"),
            P("shard", None),
            P("shard", None),
        ),
        out_specs=(
            P("shard", None),
            P("shard", None),
            P("shard", None),
            P("shard", None),
            P("shard", None),
            P("shard", "rep"),
            P("shard", "rep"),
            P("shard", "rep"),
            P("shard", "rep"),
            P("shard", "rep"),
            P("shard", "rep"),
            P("shard", "rep"),
            P("shard", "rep"),
            P("shard", "rep"),
            P("shard", "rep"),
        ),
        check_vma=False,
    )
```

```python
import jax
import jax.numpy as jnp
from jax import lax
from jax.sharding import PartitionSpec as P

rate_outer = 0.7
decay_moment = 0.9


def project(basis, matrix):
    return lax.dot_general(
        basis,
        matrix,
        (((0,), (0,)), ((), ())),
        precision=lax.Precision.HIGHEST,
        preferred_element_type=jnp.float32,
    )


def rebuild(basis, coeff):
    return jnp.dot(
        basis, coeff, precision=lax.Precision.HIGHEST, preferred_element_type=jnp.float32
    )


def nesterov(outer, moment, delta):
    moment_new = decay_moment * moment + delta
    master = outer - rate_outer * (delta + decay_moment * moment_new)
    return (master.astype(jnp.bfloat16), master, moment_new)


def owner_blocks(a, n):
    w = a.shape[1] // n
    return [a[:, j * w : (j + 1) * w] for j in range(n)]


def gather_all(y, axis_name, n):
    return lax.all_to_all(jnp.broadcast_to(y[None], (n,) + y.shape), axis_name, 0, 0, tiled=True)


def on_device(
    inner_wqkv,
    inner_w1,
    inner_w3,
    inner_wo,
    inner_w2,
    outer_wqkv,
    outer_w1,
    outer_w3,
    outer_wo,
    outer_w2,
    moment_wqkv,
    moment_w1,
    moment_w3,
    moment_wo,
    moment_w2,
    basis_wo,
    basis_w2,
):
    n = lax.axis_size("rep")
    w_qkv = outer_wqkv.shape[1]
    w_ff = outer_w1.shape[1]
    w_o = outer_wo.shape[1]
    w_2 = outer_w2.shape[1]
    rows = inner_wqkv.shape[1]
    rows_2 = outer_w2.shape[0]

    po_b = owner_blocks(project(basis_wo, inner_wo[0]), n)
    p2_b = owner_blocks(project(basis_w2, inner_w2[0]), n)
    coef_send = jnp.stack([jnp.concatenate([po_b[j], p2_b[j]], axis=1) for j in range(n)])
    part = jnp.sum(lax.all_to_all(coef_send, "rep", 0, 0, tiled=True), axis=0)
    own = jnp.concatenate([project(basis_wo, outer_wo), project(basis_w2, outer_w2)], axis=1)
    coeff = jnp.sum(lax.all_gather(own - part / n, "shard", axis=0, tiled=False), axis=0)

    qkv_b = owner_blocks(inner_wqkv[0], n)
    one_b = owner_blocks(inner_w1[0], n)
    three_b = owner_blocks(inner_w3[0], n)
    send = jnp.stack([jnp.concatenate([qkv_b[j], one_b[j], three_b[j]], axis=1) for j in range(n)])
    summed = jnp.sum(lax.all_to_all(send, "rep", 0, 0, tiled=True), axis=0)

    d_qkv = outer_wqkv - summed[:, :w_qkv] / n
    d_one = outer_w1 - summed[:, w_qkv : w_qkv + w_ff] / n
    d_three = outer_w3 - summed[:, w_qkv + w_ff :] / n
    a0, b0, c0 = nesterov(outer_wqkv, moment_wqkv, d_qkv)
    a1, b1, c1 = nesterov(outer_w1, moment_w1, d_one)
    a3, b3, c3 = nesterov(outer_w3, moment_w3, d_three)
    d_out = rebuild(basis_wo, coeff[:, :w_o])
    d_down = rebuild(basis_w2, coeff[:, w_o:])
    ao, bo, co = nesterov(outer_wo, moment_wo, d_out)
    a2, b2, c2 = nesterov(outer_w2, moment_w2, d_down)

    dense_w = gather_all(jnp.concatenate([a0, a1, a3], axis=1), "rep", n)
    q = rows_2 // rows
    low_w = gather_all(
        jnp.concatenate([ao] + [a2[k * rows : (k + 1) * rows] for k in range(q)], axis=1), "rep", n
    )
    o1 = w_qkv
    o3 = o1 + w_ff
    weights_wqkv = jnp.concatenate([dense_w[j, :, :o1] for j in range(n)], axis=1)
    weights_w1 = jnp.concatenate([dense_w[j, :, o1:o3] for j in range(n)], axis=1)
    weights_w3 = jnp.concatenate([dense_w[j, :, o3:] for j in range(n)], axis=1)
    weights_wo = jnp.concatenate([low_w[j, :, :w_o] for j in range(n)], axis=1)
    weights_w2 = jnp.concatenate(
        [
            jnp.concatenate(
                [low_w[j, :, w_o + k * w_2 : w_o + (k + 1) * w_2] for k in range(q)], axis=0
            )
            for j in range(n)
        ],
        axis=1,
    )
    return (
        weights_wqkv,
        weights_w1,
        weights_w3,
        weights_wo,
        weights_w2,
        b0,
        b1,
        b3,
        bo,
        b2,
        c0,
        c1,
        c3,
        co,
        c2,
    )


def solution(mesh):
    return jax.shard_map(
        on_device,
        mesh=mesh,
        in_specs=(
            P("rep", "shard", None),
            P("rep", "shard", None),
            P("rep", "shard", None),
            P("rep", "shard", None),
            P("rep", "shard", None),
            P("shard", "rep"),
            P("shard", "rep"),
            P("shard", "rep"),
            P("shard", "rep"),
            P("shard", "rep"),
            P("shard", "rep"),
            P("shard", "rep"),
            P("shard", "rep"),
            P("shard", "rep"),
            P("shard", "rep"),
            P("shard", None),
            P("shard", None),
        ),
        out_specs=(
            P("shard", None),
            P("shard", None),
            P("shard", None),
            P("shard", None),
            P("shard", None),
            P("shard", "rep"),
            P("shard", "rep"),
            P("shard", "rep"),
            P("shard", "rep"),
            P("shard", "rep"),
            P("shard", "rep"),
            P("shard", "rep"),
            P("shard", "rep"),
            P("shard", "rep"),
            P("shard", "rep"),
        ),
        check_vma=False,
    )
```

```python
import jax
import jax.numpy as jnp
from jax import lax
from jax.sharding import PartitionSpec as P

rate_outer = 0.7
decay_moment = 0.9


def project(basis, matrix):
    return lax.dot_general(
        basis,
        matrix,
        (((0,), (0,)), ((), ())),
        precision=lax.Precision.HIGHEST,
        preferred_element_type=jnp.float32,
    )


def rebuild(basis, coeff):
    return jnp.dot(
        basis, coeff, precision=lax.Precision.HIGHEST, preferred_element_type=jnp.float32
    )


def nesterov(outer, moment, delta):
    moment_new = decay_moment * moment + delta
    master = outer - rate_outer * (delta + decay_moment * moment_new)
    return (master.astype(jnp.bfloat16), master, moment_new)


def owner_blocks(a, n):
    w = a.shape[1] // n
    return [a[:, j * w : (j + 1) * w] for j in range(n)]


def gather_all(y, axis_name, n):
    return lax.all_to_all(jnp.broadcast_to(y[None], (n,) + y.shape), axis_name, 0, 0, tiled=True)


def on_device(
    inner_wqkv,
    inner_w1,
    inner_w3,
    inner_wo,
    inner_w2,
    outer_wqkv,
    outer_w1,
    outer_w3,
    outer_wo,
    outer_w2,
    moment_wqkv,
    moment_w1,
    moment_w3,
    moment_wo,
    moment_w2,
    basis_wo,
    basis_w2,
):
    n = lax.axis_size("rep")
    w_qkv = outer_wqkv.shape[1]
    w_ff = outer_w1.shape[1]
    w_o = outer_wo.shape[1]
    w_2 = outer_w2.shape[1]
    rows = inner_wqkv.shape[1]
    rows_2 = outer_w2.shape[0]
    rank = basis_wo.shape[1]
    width = w_qkv + 2 * w_ff
    w_c = w_o + w_2
    k_c = width // w_c
    r_c = rank // k_c

    qkv_b = owner_blocks(inner_wqkv[0], n)
    one_b = owner_blocks(inner_w1[0], n)
    three_b = owner_blocks(inner_w3[0], n)
    po_b = owner_blocks(project(basis_wo, inner_wo[0]), n)
    p2_b = owner_blocks(project(basis_w2, inner_w2[0]), n)
    send = []
    for j in range(n):
        part = jnp.concatenate([po_b[j], p2_b[j]], axis=1)
        folded = jnp.concatenate([part[k * r_c : (k + 1) * r_c] for k in range(k_c)], axis=1)
        dense = jnp.concatenate([qkv_b[j], one_b[j], three_b[j]], axis=1)
        send.append(jnp.concatenate([dense, folded], axis=0))
    got = lax.all_to_all(jnp.stack(send), "rep", 0, 0, tiled=True)
    total = got[0]
    for g in range(1, n):
        total = total + got[g]

    summed = total[:rows]
    folded = total[rows:]
    part = jnp.concatenate([folded[:, k * w_c : (k + 1) * w_c] for k in range(k_c)], axis=0)
    own = jnp.concatenate([project(basis_wo, outer_wo), project(basis_w2, outer_w2)], axis=1)
    coeff = jnp.sum(lax.all_gather(own - part / n, "shard", axis=0, tiled=False), axis=0)

    d_qkv = outer_wqkv - summed[:, :w_qkv] / n
    d_one = outer_w1 - summed[:, w_qkv : w_qkv + w_ff] / n
    d_three = outer_w3 - summed[:, w_qkv + w_ff :] / n
    a0, b0, c0 = nesterov(outer_wqkv, moment_wqkv, d_qkv)
    a1, b1, c1 = nesterov(outer_w1, moment_w1, d_one)
    a3, b3, c3 = nesterov(outer_w3, moment_w3, d_three)
    d_out = rebuild(basis_wo, coeff[:, :w_o])
    d_down = rebuild(basis_w2, coeff[:, w_o:])
    ao, bo, co = nesterov(outer_wo, moment_wo, d_out)
    a2, b2, c2 = nesterov(outer_w2, moment_w2, d_down)

    dense_w = gather_all(jnp.concatenate([a0, a1, a3], axis=1), "rep", n)
    low = lax.all_to_all(
        jnp.broadcast_to(jnp.concatenate([ao, a2], axis=0)[None], (n, rows + rows_2, w_o)),
        "rep",
        0,
        2,
        tiled=True,
    )[0]
    o1 = w_qkv
    o3 = o1 + w_ff
    weights_wqkv = jnp.concatenate([dense_w[j, :, :o1] for j in range(n)], axis=1)
    weights_w1 = jnp.concatenate([dense_w[j, :, o1:o3] for j in range(n)], axis=1)
    weights_w3 = jnp.concatenate([dense_w[j, :, o3:] for j in range(n)], axis=1)
    weights_wo = low[:rows]
    weights_w2 = low[rows:]
    return (
        weights_wqkv,
        weights_w1,
        weights_w3,
        weights_wo,
        weights_w2,
        b0,
        b1,
        b3,
        bo,
        b2,
        c0,
        c1,
        c3,
        co,
        c2,
    )


def solution(mesh):
    return jax.shard_map(
        on_device,
        mesh=mesh,
        in_specs=(
            P("rep", "shard", None),
            P("rep", "shard", None),
            P("rep", "shard", None),
            P("rep", "shard", None),
            P("rep", "shard", None),
            P("shard", "rep"),
            P("shard", "rep"),
            P("shard", "rep"),
            P("shard", "rep"),
            P("shard", "rep"),
            P("shard", "rep"),
            P("shard", "rep"),
            P("shard", "rep"),
            P("shard", "rep"),
            P("shard", "rep"),
            P("shard", None),
            P("shard", None),
        ),
        out_specs=(
            P("shard", None),
            P("shard", None),
            P("shard", None),
            P("shard", None),
            P("shard", None),
            P("shard", "rep"),
            P("shard", "rep"),
            P("shard", "rep"),
            P("shard", "rep"),
            P("shard", "rep"),
            P("shard", "rep"),
            P("shard", "rep"),
            P("shard", "rep"),
            P("shard", "rep"),
            P("shard", "rep"),
        ),
        check_vma=False,
    )
```

```python
import jax
import jax.numpy as jnp
from jax import lax
from jax.sharding import PartitionSpec as P

rate_outer = 0.7
decay_moment = 0.9


def project(basis, matrix):
    return lax.dot_general(
        basis,
        matrix,
        (((0,), (0,)), ((), ())),
        precision=lax.Precision.HIGHEST,
        preferred_element_type=jnp.float32,
    )


def rebuild(basis, coeff):
    return jnp.dot(
        basis, coeff, precision=lax.Precision.HIGHEST, preferred_element_type=jnp.float32
    )


def nesterov(outer, moment, delta):
    moment_new = decay_moment * moment + delta
    master = outer - rate_outer * (delta + decay_moment * moment_new)
    return (master.astype(jnp.bfloat16), master, moment_new)


def owner_blocks(a, n):
    w = a.shape[1] // n
    return [a[:, j * w : (j + 1) * w] for j in range(n)]


def from_owners(g):
    n, r, w = g.shape
    return g.transpose(1, 0, 2).reshape(r, n * w)


def gather_all(y, axis_name, n):
    return lax.all_to_all(jnp.broadcast_to(y[None], (n,) + y.shape), axis_name, 0, 0, tiled=True)


def on_device(
    inner_wqkv,
    inner_w1,
    inner_w3,
    inner_wo,
    inner_w2,
    outer_wqkv,
    outer_w1,
    outer_w3,
    outer_wo,
    outer_w2,
    moment_wqkv,
    moment_w1,
    moment_w3,
    moment_wo,
    moment_w2,
    basis_wo,
    basis_w2,
):
    n = lax.axis_size("rep")
    w_qkv = outer_wqkv.shape[1]
    w_ff = outer_w1.shape[1]
    w_o = outer_wo.shape[1]
    w_2 = outer_w2.shape[1]
    rows = inner_wqkv.shape[1]
    rows_2 = outer_w2.shape[0]
    rank = basis_wo.shape[1]
    width = w_qkv + 2 * w_ff
    w_c = w_o + w_2
    k_c = width // w_c
    r_c = rank // k_c

    qkv_b = owner_blocks(inner_wqkv[0], n)
    one_b = owner_blocks(inner_w1[0], n)
    three_b = owner_blocks(inner_w3[0], n)
    po_b = owner_blocks(project(basis_wo, inner_wo[0]), n)
    p2_b = owner_blocks(project(basis_w2, inner_w2[0]), n)
    send = []
    for j in range(n):
        part = jnp.concatenate([po_b[j], p2_b[j]], axis=1)
        folded = jnp.concatenate([part[k * r_c : (k + 1) * r_c] for k in range(k_c)], axis=1)
        dense = jnp.concatenate([qkv_b[j], one_b[j], three_b[j]], axis=1)
        send.append(jnp.concatenate([dense, folded], axis=0))
    got = lax.all_to_all(jnp.stack(send), "rep", 0, 0, tiled=True)
    total = got[0]
    for g in range(1, n):
        total = total + got[g]

    summed = total[:rows]
    folded = total[rows:]
    part = jnp.concatenate([folded[:, k * w_c : (k + 1) * w_c] for k in range(k_c)], axis=0)
    own = jnp.concatenate([project(basis_wo, outer_wo), project(basis_w2, outer_w2)], axis=1)
    coeff = jnp.sum(lax.all_gather(own - part / n, "shard", axis=0, tiled=False), axis=0)

    d_qkv = outer_wqkv - summed[:, :w_qkv] / n
    d_one = outer_w1 - summed[:, w_qkv : w_qkv + w_ff] / n
    d_three = outer_w3 - summed[:, w_qkv + w_ff :] / n
    a0, b0, c0 = nesterov(outer_wqkv, moment_wqkv, d_qkv)
    a1, b1, c1 = nesterov(outer_w1, moment_w1, d_one)
    a3, b3, c3 = nesterov(outer_w3, moment_w3, d_three)
    d_out = rebuild(basis_wo, coeff[:, :w_o])
    d_down = rebuild(basis_w2, coeff[:, w_o:])
    ao, bo, co = nesterov(outer_wo, moment_wo, d_out)
    a2, b2, c2 = nesterov(outer_w2, moment_w2, d_down)

    dense_w = gather_all(jnp.concatenate([a0, a1, a3], axis=1), "rep", n)
    low_w = gather_all(jnp.concatenate([ao, a2], axis=0), "rep", n)
    o1 = w_qkv
    o3 = o1 + w_ff
    weights_wqkv = from_owners(dense_w[:, :, :o1])
    weights_w1 = from_owners(dense_w[:, :, o1:o3])
    weights_w3 = from_owners(dense_w[:, :, o3:])
    weights_wo = from_owners(low_w[:, :rows])
    weights_w2 = from_owners(low_w[:, rows:])
    return (
        weights_wqkv,
        weights_w1,
        weights_w3,
        weights_wo,
        weights_w2,
        b0,
        b1,
        b3,
        bo,
        b2,
        c0,
        c1,
        c3,
        co,
        c2,
    )


def solution(mesh):
    return jax.shard_map(
        on_device,
        mesh=mesh,
        in_specs=(
            P("rep", "shard", None),
            P("rep", "shard", None),
            P("rep", "shard", None),
            P("rep", "shard", None),
            P("rep", "shard", None),
            P("shard", "rep"),
            P("shard", "rep"),
            P("shard", "rep"),
            P("shard", "rep"),
            P("shard", "rep"),
            P("shard", "rep"),
            P("shard", "rep"),
            P("shard", "rep"),
            P("shard", "rep"),
            P("shard", "rep"),
            P("shard", None),
            P("shard", None),
        ),
        out_specs=(
            P("shard", None),
            P("shard", None),
            P("shard", None),
            P("shard", None),
            P("shard", None),
            P("shard", "rep"),
            P("shard", "rep"),
            P("shard", "rep"),
            P("shard", "rep"),
            P("shard", "rep"),
            P("shard", "rep"),
            P("shard", "rep"),
            P("shard", "rep"),
            P("shard", "rep"),
            P("shard", "rep"),
        ),
        check_vma=False,
    )
```

```python
import jax
import jax.numpy as jnp
from jax import lax
from jax.sharding import PartitionSpec as P

rate_outer = 0.7
decay_moment = 0.9


def project(basis, matrix):
    return lax.dot_general(
        basis,
        matrix,
        (((0,), (0,)), ((), ())),
        precision=lax.Precision.HIGHEST,
        preferred_element_type=jnp.float32,
    )


def rebuild(basis, coeff):
    return jnp.dot(
        basis, coeff, precision=lax.Precision.HIGHEST, preferred_element_type=jnp.float32
    )


def nesterov(outer, moment, delta):
    moment_new = decay_moment * moment + delta
    master = outer - rate_outer * (delta + decay_moment * moment_new)
    return (master.astype(jnp.bfloat16), master, moment_new)


def owner_blocks(a, n):
    w = a.shape[1] // n
    return [a[:, j * w : (j + 1) * w] for j in range(n)]


def gather_all(y, axis_name, n):
    return lax.all_to_all(jnp.broadcast_to(y[None], (n,) + y.shape), axis_name, 0, 0, tiled=True)


def on_device(
    inner_wqkv,
    inner_w1,
    inner_w3,
    inner_wo,
    inner_w2,
    outer_wqkv,
    outer_w1,
    outer_w3,
    outer_wo,
    outer_w2,
    moment_wqkv,
    moment_w1,
    moment_w3,
    moment_wo,
    moment_w2,
    basis_wo,
    basis_w2,
):
    n = lax.axis_size("rep")
    w_qkv = outer_wqkv.shape[1]
    w_ff = outer_w1.shape[1]
    w_o = outer_wo.shape[1]
    w_2 = outer_w2.shape[1]
    rows = inner_wqkv.shape[1]
    rows_2 = outer_w2.shape[0]
    rank = basis_wo.shape[1]
    width = w_qkv + 2 * w_ff
    w_c = w_o + w_2
    k_c = width // w_c
    r_c = rank // k_c

    qkv_b = owner_blocks(inner_wqkv[0], n)
    one_b = owner_blocks(inner_w1[0], n)
    three_b = owner_blocks(inner_w3[0], n)
    po_b = owner_blocks(project(basis_wo, inner_wo[0]), n)
    p2_b = owner_blocks(project(basis_w2, inner_w2[0]), n)
    send = []
    for j in range(n):
        part = jnp.concatenate([po_b[j], p2_b[j]], axis=1)
        folded = jnp.concatenate([part[k * r_c : (k + 1) * r_c] for k in range(k_c)], axis=1)
        dense = jnp.concatenate([qkv_b[j], one_b[j], three_b[j]], axis=1)
        send.append(jnp.concatenate([dense, folded], axis=0))
    got = lax.all_to_all(jnp.stack(send), "rep", 0, 0, tiled=True)
    total = got[0]
    for g in range(1, n):
        total = total + got[g]

    summed = total[:rows]
    folded = total[rows:]
    part = jnp.concatenate([folded[:, k * w_c : (k + 1) * w_c] for k in range(k_c)], axis=0)
    own = jnp.concatenate([project(basis_wo, outer_wo), project(basis_w2, outer_w2)], axis=1)
    coeff = jnp.sum(lax.all_gather(own - part / n, "shard", axis=0, tiled=False), axis=0)

    d_qkv = outer_wqkv - summed[:, :w_qkv] / n
    d_one = outer_w1 - summed[:, w_qkv : w_qkv + w_ff] / n
    d_three = outer_w3 - summed[:, w_qkv + w_ff :] / n
    a0, b0, c0 = nesterov(outer_wqkv, moment_wqkv, d_qkv)
    a1, b1, c1 = nesterov(outer_w1, moment_w1, d_one)
    a3, b3, c3 = nesterov(outer_w3, moment_w3, d_three)
    d_out = rebuild(basis_wo, coeff[:, :w_o])
    d_down = rebuild(basis_w2, coeff[:, w_o:])
    ao, bo, co = nesterov(outer_wo, moment_wo, d_out)
    a2, b2, c2 = nesterov(outer_w2, moment_w2, d_down)

    dense_w = gather_all(jnp.concatenate([a0, a1, a3], axis=1), "rep", n)
    q = rows_2 // rows
    low_w = gather_all(
        jnp.concatenate([ao] + [a2[k * rows : (k + 1) * rows] for k in range(q)], axis=1), "rep", n
    )
    o1 = w_qkv
    o3 = o1 + w_ff
    weights_wqkv = jnp.concatenate([dense_w[j, :, :o1] for j in range(n)], axis=1)
    weights_w1 = jnp.concatenate([dense_w[j, :, o1:o3] for j in range(n)], axis=1)
    weights_w3 = jnp.concatenate([dense_w[j, :, o3:] for j in range(n)], axis=1)
    weights_wo = jnp.concatenate([low_w[j, :, :w_o] for j in range(n)], axis=1)
    weights_w2 = jnp.concatenate(
        [
            jnp.concatenate(
                [low_w[j, :, w_o + k * w_2 : w_o + (k + 1) * w_2] for k in range(q)], axis=0
            )
            for j in range(n)
        ],
        axis=1,
    )
    return (
        weights_wqkv,
        weights_w1,
        weights_w3,
        weights_wo,
        weights_w2,
        b0,
        b1,
        b3,
        bo,
        b2,
        c0,
        c1,
        c3,
        co,
        c2,
    )


def solution(mesh):
    return jax.shard_map(
        on_device,
        mesh=mesh,
        in_specs=(
            P("rep", "shard", None),
            P("rep", "shard", None),
            P("rep", "shard", None),
            P("rep", "shard", None),
            P("rep", "shard", None),
            P("shard", "rep"),
            P("shard", "rep"),
            P("shard", "rep"),
            P("shard", "rep"),
            P("shard", "rep"),
            P("shard", "rep"),
            P("shard", "rep"),
            P("shard", "rep"),
            P("shard", "rep"),
            P("shard", "rep"),
            P("shard", None),
            P("shard", None),
        ),
        out_specs=(
            P("shard", None),
            P("shard", None),
            P("shard", None),
            P("shard", None),
            P("shard", None),
            P("shard", "rep"),
            P("shard", "rep"),
            P("shard", "rep"),
            P("shard", "rep"),
            P("shard", "rep"),
            P("shard", "rep"),
            P("shard", "rep"),
            P("shard", "rep"),
            P("shard", "rep"),
            P("shard", "rep"),
        ),
        check_vma=False,
    )
```

```python
import jax
import jax.numpy as jnp
from jax import lax
from jax.sharding import PartitionSpec as P

rate_outer = 0.7
decay_moment = 0.9


def project(basis, matrix):
    return lax.dot_general(
        basis,
        matrix,
        (((0,), (0,)), ((), ())),
        precision=lax.Precision.HIGHEST,
        preferred_element_type=jnp.float32,
    )


def rebuild(basis, coeff):
    return jnp.dot(
        basis, coeff, precision=lax.Precision.HIGHEST, preferred_element_type=jnp.float32
    )


def nesterov(outer, moment, delta):
    moment_new = decay_moment * moment + delta
    master = outer - rate_outer * (delta + decay_moment * moment_new)
    return (master.astype(jnp.bfloat16), master, moment_new)


def owner_blocks(a, n):
    w = a.shape[1] // n
    return [a[:, j * w : (j + 1) * w] for j in range(n)]


def gather_all(y, axis_name, n):
    return lax.all_to_all(jnp.broadcast_to(y[None], (n,) + y.shape), axis_name, 0, 0, tiled=True)


def on_device(
    inner_wqkv,
    inner_w1,
    inner_w3,
    inner_wo,
    inner_w2,
    outer_wqkv,
    outer_w1,
    outer_w3,
    outer_wo,
    outer_w2,
    moment_wqkv,
    moment_w1,
    moment_w3,
    moment_wo,
    moment_w2,
    basis_wo,
    basis_w2,
):
    n = lax.axis_size("rep")
    w_qkv = outer_wqkv.shape[1]
    w_ff = outer_w1.shape[1]
    w_o = outer_wo.shape[1]
    w_2 = outer_w2.shape[1]
    rows = inner_wqkv.shape[1]
    rows_2 = outer_w2.shape[0]
    rank = basis_wo.shape[1]
    width = w_qkv + 2 * w_ff
    w_c = w_o + w_2
    k_c = width // w_c
    r_c = rank // k_c

    qkv_b = owner_blocks(inner_wqkv[0], n)
    one_b = owner_blocks(inner_w1[0], n)
    three_b = owner_blocks(inner_w3[0], n)
    po_b = owner_blocks(project(basis_wo, inner_wo[0]), n)
    p2_b = owner_blocks(project(basis_w2, inner_w2[0]), n)
    send = []
    for j in range(n):
        part = jnp.concatenate([po_b[j], p2_b[j]], axis=1)
        folded = jnp.concatenate([part[k * r_c : (k + 1) * r_c] for k in range(k_c)], axis=1)
        dense = jnp.concatenate([qkv_b[j], one_b[j], three_b[j]], axis=1)
        send.append(jnp.concatenate([dense, folded], axis=0))
    got = lax.all_to_all(jnp.stack(send), "rep", 0, 0, tiled=True)
    total = got[0]
    for g in range(1, n):
        total = total + got[g]

    summed = total[:rows]
    folded = total[rows:]
    part = jnp.concatenate([folded[:, k * w_c : (k + 1) * w_c] for k in range(k_c)], axis=0)
    own = jnp.concatenate([project(basis_wo, outer_wo), project(basis_w2, outer_w2)], axis=1)
    coeff = jnp.sum(gather_all(own - part / n, "shard", lax.axis_size("shard")), axis=0)

    d_qkv = outer_wqkv - summed[:, :w_qkv] / n
    d_one = outer_w1 - summed[:, w_qkv : w_qkv + w_ff] / n
    d_three = outer_w3 - summed[:, w_qkv + w_ff :] / n
    a0, b0, c0 = nesterov(outer_wqkv, moment_wqkv, d_qkv)
    a1, b1, c1 = nesterov(outer_w1, moment_w1, d_one)
    a3, b3, c3 = nesterov(outer_w3, moment_w3, d_three)
    d_out = rebuild(basis_wo, coeff[:, :w_o])
    d_down = rebuild(basis_w2, coeff[:, w_o:])
    ao, bo, co = nesterov(outer_wo, moment_wo, d_out)
    a2, b2, c2 = nesterov(outer_w2, moment_w2, d_down)

    dense_w = gather_all(jnp.concatenate([a0, a1, a3], axis=1), "rep", n)
    q = rows_2 // rows
    low_w = gather_all(
        jnp.concatenate([ao] + [a2[k * rows : (k + 1) * rows] for k in range(q)], axis=1), "rep", n
    )
    o1 = w_qkv
    o3 = o1 + w_ff
    weights_wqkv = jnp.concatenate([dense_w[j, :, :o1] for j in range(n)], axis=1)
    weights_w1 = jnp.concatenate([dense_w[j, :, o1:o3] for j in range(n)], axis=1)
    weights_w3 = jnp.concatenate([dense_w[j, :, o3:] for j in range(n)], axis=1)
    weights_wo = jnp.concatenate([low_w[j, :, :w_o] for j in range(n)], axis=1)
    weights_w2 = jnp.concatenate(
        [
            jnp.concatenate(
                [low_w[j, :, w_o + k * w_2 : w_o + (k + 1) * w_2] for k in range(q)], axis=0
            )
            for j in range(n)
        ],
        axis=1,
    )
    return (
        weights_wqkv,
        weights_w1,
        weights_w3,
        weights_wo,
        weights_w2,
        b0,
        b1,
        b3,
        bo,
        b2,
        c0,
        c1,
        c3,
        co,
        c2,
    )


def solution(mesh):
    return jax.shard_map(
        on_device,
        mesh=mesh,
        in_specs=(
            P("rep", "shard", None),
            P("rep", "shard", None),
            P("rep", "shard", None),
            P("rep", "shard", None),
            P("rep", "shard", None),
            P("shard", "rep"),
            P("shard", "rep"),
            P("shard", "rep"),
            P("shard", "rep"),
            P("shard", "rep"),
            P("shard", "rep"),
            P("shard", "rep"),
            P("shard", "rep"),
            P("shard", "rep"),
            P("shard", "rep"),
            P("shard", None),
            P("shard", None),
        ),
        out_specs=(
            P("shard", None),
            P("shard", None),
            P("shard", None),
            P("shard", None),
            P("shard", None),
            P("shard", "rep"),
            P("shard", "rep"),
            P("shard", "rep"),
            P("shard", "rep"),
            P("shard", "rep"),
            P("shard", "rep"),
            P("shard", "rep"),
            P("shard", "rep"),
            P("shard", "rep"),
            P("shard", "rep"),
        ),
        check_vma=False,
    )
```
